256 devices in a mesh: sub: 16 (over z, core), fr: 16 (over y, x).
Axes of the slice: x: 4, y: 4, z: 8, core: 2. Of those that a mesh axis runs over, the one named last changes fastest.
Arguments:
- front_leaf: bfloat16 [32768, 2048], P(('sub', 'fr')), as said below
- shares_one: float32 [32768, 384], P(('sub', 'fr')), as said below
- shares_two: float32 [32768, 384], P(('sub', 'fr')), as said below
- map_leaf: int32 [16, 13], P('sub'), may hold values from 0 to 15, as said below
- map_mid: int32 [8, 13], replicated, may hold values from 0 to 15, as said below
Outputs:
- leaf_panel: float32 [32768, 384], P(('sub', 'fr'))
- middle_panel: float32 [32768, 384], P(('sub', 'fr'))
- top_panel: float32 [32768, 384], P(('sub', 'fr'))
- contribution: float32 [32768, 1664], P(('sub', 'fr'))
The draws below stay inside these ranges and needn't reach their ends.
Inputs may be any that keep to these rules, and one draw needn't show every extreme that they name: `front_leaf`: each block of 2048 rows is a symmetric positive definite front. `shares_one`: in each block of 2048 rows the first 384 rows are symmetric; with the extended contributions every middle front is positive definite. `shares_two`: in each block of 2048 rows the first 384 rows are symmetric; with the extended contributions every top front is positive definite. `map_leaf`: each row lists 13 different blocks; rows 2q and 2q+1 together name every block of their parent. `map_mid`: each row lists 13 different blocks; rows 2r and 2r+1 together name every block of their parent.
All inputs are finite; a program needn't handle non-finite values.
Results may differ from the reference program's by a relative error of at most 0.0003.
Values sent between devices are 32-bit elements; how exact they have to be, the bound alone decides.
No kernel may reach another device: no remote copies, remote signals or barrier semaphores. Data moves between devices by JAX's collectives and lax.ppermute only.
A program may use at most 128 MiB of HBM per device.

```python
import math
import jax
import jax.numpy as jnp
from jax import lax

F = 2048
BLK = 128
P_SIZE = 384
NFB = 16
NPB = 3
NU = 13
N_SUB = 16


def draw_front_leaf(key, part):
    key_off, key_gain = jax.random.split(key, 2)
    raw_draw = jax.random.uniform(key_off, (N_SUB, F, F), jnp.float32, -1.7, 1.7)
    symmetric = (raw_draw + jnp.swapaxes(raw_draw, 1, 2)) * 0.7071
    level_values = jax.random.uniform(key_gain, (N_SUB, F), jnp.float32, 0.0, 1.0)
    identity = jnp.eye(F, dtype=jnp.float32)
    diagonal = math.sqrt(F) * (2.36 + 0.6 * level_values)
    result = symmetric * (1.0 - identity) + diagonal[:, :, None] * identity
    return result.reshape(N_SUB * F, F).astype(jnp.bfloat16)


def share_draw(key, members):
    key_top, key_gain, key_rest = jax.random.split(key, 3)
    spread = 1.0 / math.sqrt(members)
    upper_part = jax.random.uniform(key_top, (N_SUB, P_SIZE, P_SIZE), jnp.float32, -0.85 * spread, 0.85 * spread)
    pivot_part = (upper_part + jnp.swapaxes(upper_part, 1, 2)) * 0.7071
    gain_values = jnp.exp(jax.random.uniform(key_gain, (N_SUB, P_SIZE), jnp.float32, math.log(1.25), math.log(3.0)))
    identity = jnp.eye(P_SIZE, dtype=jnp.float32)
    pivot_part = pivot_part * (1.0 - identity) + 1.15 / members * math.sqrt(F) * gain_values[:, :, None] * identity
    lower_rows = jax.random.uniform(key_rest, (N_SUB, F - P_SIZE, P_SIZE), jnp.float32, -0.5 * spread, 0.5 * spread)
    return jnp.concatenate([pivot_part, lower_rows], axis=1).reshape(N_SUB * F, P_SIZE)


def draw_shares_one(key, part):
    return share_draw(jax.random.fold_in(key, 3), 2)


def draw_shares_two(key, part):
    return share_draw(jax.random.fold_in(key, 5), 4)


def pair_maps(key, pairs):

    def one_pair(pair_key):
        key_a, key_b, key_c = jax.random.split(pair_key, 3)
        scores_a = jax.random.permutation(key_a, NFB).astype(jnp.int32)
        unused_a, keep_a = lax.top_k(scores_a, NU)
        chosen_a = jnp.zeros((NFB,), jnp.int32).at[keep_a].set(1)
        scores_b = jax.random.permutation(key_b, NFB).astype(jnp.int32) + NFB * (1 - chosen_a)
        unused_b, keep_b = lax.top_k(scores_b, NU)
        map_a = keep_a.astype(jnp.int32)
        map_b = keep_b.astype(jnp.int32)
        flipped = jax.random.randint(key_c, (), 0, 2)
        lower_map = jnp.where(flipped == 0, map_a, map_b)
        upper_map = jnp.where(flipped == 0, map_b, map_a)
        return jnp.stack([lower_map, upper_map])
    stacked = jax.vmap(one_pair)(jax.random.split(key, pairs))
    return stacked.reshape(2 * pairs, NU).astype(jnp.int32)


def draw_map_leaf(key, part):
    return pair_maps(jax.random.fold_in(key, 11), N_SUB // 2)


def draw_map_mid(key, part):
    return pair_maps(jax.random.fold_in(key, 12), N_SUB // 4)


def setup_inputs(seed: int = 0) -> dict:
    key_list = jax.random.split(jax.random.key(seed), 6)
    return {
        "front_leaf": draw_front_leaf(jax.random.fold_in(key_list[5], 71), 0),
        "shares_one": draw_shares_one(jax.random.fold_in(key_list[5], 71), 0),
        "shares_two": draw_shares_two(jax.random.fold_in(key_list[5], 71), 0),
        "map_leaf": draw_map_leaf(jax.random.fold_in(key_list[5], 71), 0),
        "map_mid": draw_map_mid(jax.random.fold_in(key_list[5], 71), 0),
    }


HIGH = lax.Precision.HIGHEST

def eliminate(front):
    row_ids = jnp.arange(F)
    panels = []
    for block_index in range(NPB):
        block_low = block_index * BLK
        column = front[:, block_low:block_low + BLK]
        lower_block = jnp.linalg.cholesky(column[block_low:block_low + BLK])
        solved = lax.linalg.triangular_solve(lower_block, column, left_side=False, lower=True, transpose_a=True)
        below = jnp.where((row_ids >= block_low + BLK)[:, None], solved, 0.0)
        panels.append(below.at[block_low:block_low + BLK].set(lower_block))
        front = front - jnp.dot(below.astype(jnp.float32), below.T.astype(jnp.float32), precision=HIGH, preferred_element_type=jnp.float32)
    return (jnp.concatenate(panels, axis=1), front)

def make_table(block_map):
    padded = jnp.concatenate([jnp.full((NPB,), -1, jnp.int32), block_map.astype(jnp.int32)])
    return (padded[:, None] == jnp.arange(NFB, dtype=jnp.int32)[None, :]).astype(jnp.float32)

def extend_add(front, block_map):
    block_table = make_table(block_map)
    tiles = front.reshape(NFB, BLK, NFB, BLK)
    placed = jnp.einsum('aibj,ae,bf->eifj', tiles, block_table, block_table, precision=HIGH)
    return placed.reshape(F, F)

def make_parent(children, block_maps, shares):
    summed = jnp.sum(shares, axis=0)
    parent_front = jnp.pad(summed, ((0, 0), (0, F - P_SIZE)))
    for index in range(2):
        parent_front = parent_front + extend_add(children[index], block_maps[index])
    return parent_front

def one_quad(items):
    leaves, shares_low, shares_high, maps_low, maps_high = items
    leaf_panels = []
    middle_panels = []
    middle_fronts = []
    for pair_index in range(2):
        children = []
        for side in range(2):
            panel_rows, child_front = eliminate(leaves[2 * pair_index + side].astype(jnp.float32))
            leaf_panels.append(panel_rows)
            children.append(child_front)
        middle_front = make_parent(children, maps_low[2 * pair_index:2 * pair_index + 2], shares_low[2 * pair_index:2 * pair_index + 2])
        panel_rows, middle_front = eliminate(middle_front)
        middle_panels.append(panel_rows)
        middle_panels.append(panel_rows)
        middle_fronts.append(middle_front)
    top_front = make_parent(middle_fronts, maps_high, shares_high)
    top_rows, top_front = eliminate(top_front)
    schur_part = jnp.where((jnp.arange(F) >= P_SIZE)[:, None], top_front[:, P_SIZE:], 0.0)
    return (jnp.stack(leaf_panels), jnp.stack(middle_panels), jnp.stack([top_rows] * 4), jnp.stack([schur_part] * 4))

def reference(front_leaf, shares_one, shares_two, map_leaf, map_mid):
    quads = N_SUB // 4
    items = (front_leaf.reshape(quads, 4, F, F), shares_one.reshape(quads, 4, F, P_SIZE), shares_two.reshape(quads, 4, F, P_SIZE), map_leaf.reshape(quads, 4, NU), map_mid.reshape(quads, 2, NU))
    leaf_panel, middle_panel, top_panel, contribution = lax.map(one_quad, items)
    return (leaf_panel.reshape(N_SUB * F, P_SIZE), middle_panel.reshape(N_SUB * F, P_SIZE), top_panel.reshape(N_SUB * F, P_SIZE), contribution.reshape(N_SUB * F, F - P_SIZE))
```

```python
import jax
import jax.numpy as jnp
from jax import lax
from jax.sharding import PartitionSpec as P

BLK = 128
P_SIZE = 384
NFB = 16
NPB = 3


HIGH = lax.Precision.HIGHEST


def partner(array, axis, stride):
    return lax.ppermute(array, axis, [(i, i ^ 1 << stride) for i in range(lax.axis_size(axis))])


def factor(columns):
    lower_block = jnp.tril(jnp.linalg.cholesky(columns[:P_SIZE]))
    solved = lax.linalg.triangular_solve(
        lower_block, columns[P_SIZE:], left_side=False, lower=True, transpose_a=True
    )
    return jnp.concatenate([lower_block, solved], axis=0)


def gather_rows(array):
    return lax.all_gather(array, "fr", axis=0, tiled=True)


def extend(rest, panel, block_map):
    parent_block = lax.axis_index("fr")
    matches = block_map == parent_block
    present = jnp.any(matches)
    child_block = NPB + jnp.argmax(matches)
    rows = lax.dynamic_slice_in_dim(rest, child_block * BLK, BLK, 0)
    panel_rows = lax.dynamic_slice_in_dim(panel, child_block * BLK, BLK, 0)
    schur = rows - jnp.dot(
        panel_rows, panel[P_SIZE:].T, precision=HIGH, preferred_element_type=jnp.float32
    )
    column_match = block_map[None, :] == jnp.arange(NFB, dtype=jnp.int32)[:, None]
    has_column = jnp.any(column_match, axis=1)
    source_column = jnp.argmax(column_match, axis=1)
    tiles = schur.reshape(BLK, NFB - NPB, BLK)
    placed = jnp.take(tiles, source_column, axis=1)
    placed = jnp.where(has_column[None, :, None] & present, placed, 0.0)
    return placed.reshape(BLK, NFB * BLK)


def level(front, row_start):
    panel = factor(gather_rows(front[:, :P_SIZE]))
    own_panel = lax.dynamic_slice_in_dim(panel, row_start, front.shape[0], 0)
    return panel, own_panel


def combine(front, shares, block_map, level_bit):
    row_start = lax.axis_index("fr") * front.shape[0]
    panel, own_panel = level(front, row_start)
    rest = gather_rows(front[:, P_SIZE:])
    piece = extend(rest, panel, block_map)
    piece = piece.at[:, :P_SIZE].add(shares)
    return own_panel, piece + partner(piece, "sub", level_bit)


def local(front_leaf, shares_one, shares_two, map_leaf, map_mid):
    row_count = front_leaf.shape[0]
    row_start = lax.axis_index("fr") * row_count
    sub_index = lax.axis_index("sub")
    shares_sum = shares_two + partner(shares_two, "sub", 0)
    leaf_panel, middle_front = combine(front_leaf.astype(jnp.float32), shares_one, map_leaf[0], 0)
    pair_map = lax.dynamic_index_in_dim(map_mid, sub_index // 2, 0, keepdims=False)
    middle_panel, top_front = combine(middle_front, shares_sum, pair_map, 1)
    panel, top_panel = level(top_front, row_start)
    schur = top_front[:, P_SIZE:] - jnp.dot(
        top_panel, panel[P_SIZE:].T, precision=HIGH, preferred_element_type=jnp.float32
    )
    row_ids = row_start + jnp.arange(row_count)
    contribution = jnp.where((row_ids >= P_SIZE)[:, None], schur, 0.0)
    return (leaf_panel, middle_panel, top_panel, contribution)


def solution(mesh):
    in_specs = (
        P(("sub", "fr"), None),
        P(("sub", "fr"), None),
        P(("sub", "fr"), None),
        P("sub", None),
        P(),
    )
    out_specs = (
        P(("sub", "fr"), None),
        P(("sub", "fr"), None),
        P(("sub", "fr"), None),
        P(("sub", "fr"), None),
    )
    return jax.shard_map(local, mesh=mesh, in_specs=in_specs, out_specs=out_specs, check_vma=False)
```

```python
import jax
import jax.numpy as jnp
from jax import lax
from jax.sharding import PartitionSpec as P

BLK = 128
P_SIZE = 384
NFB = 16
NPB = 3


HIGH = lax.Precision.HIGHEST


def partner(array, axis, stride):
    return lax.ppermute(array, axis, [(i, i ^ 1 << stride) for i in range(lax.axis_size(axis))])


def gather_rows(array):
    return lax.all_gather(array, "fr", axis=0, tiled=True)


def dot_t(left, right):
    return jnp.dot(left, right.T, precision=HIGH, preferred_element_type=jnp.float32)


def factor(columns):
    trailing = columns
    panels = []
    for block_index in range(NPB):
        block_low = block_index * BLK
        lower_block = jnp.tril(jnp.linalg.cholesky(trailing[:BLK, :BLK]))
        below = lax.linalg.triangular_solve(
            lower_block, trailing[BLK:, :BLK], left_side=False, lower=True, transpose_a=True
        )
        panels.append(
            jnp.concatenate(
                [jnp.zeros((block_low, BLK), jnp.float32), lower_block, below], axis=0
            )
        )
        if block_index < NPB - 1:
            width = trailing.shape[1] - BLK
            trailing = trailing[BLK:, BLK:] - dot_t(below, below[:width])
    return jnp.concatenate(panels, axis=1)


def block_source(block_map):
    match = block_map[None, :] == jnp.arange(NFB, dtype=jnp.int32)[:, None]
    return jnp.any(match, axis=1), jnp.argmax(match, axis=1)


def extend_columns(rest, panel, block_map):
    has, source = block_source(block_map)
    lower = panel[P_SIZE:]
    count = NFB - NPB
    picked = jnp.take(rest[P_SIZE:].reshape(count * BLK, count, BLK), source[:NPB], axis=1)
    picked_panel = jnp.take(lower.reshape(count, BLK, P_SIZE), source[:NPB], axis=0)
    schur = picked.reshape(count * BLK, P_SIZE) - dot_t(lower, picked_panel.reshape(P_SIZE, P_SIZE))
    schur = jnp.where(jnp.repeat(has[:NPB], BLK)[None, :], schur, 0.0)
    rows = jnp.take(schur.reshape(count, BLK, P_SIZE), source, axis=0)
    rows = jnp.where(has[:, None, None], rows, 0.0)
    return rows.reshape(NFB * BLK, P_SIZE)


def extend_own(rest, panel, block_map):
    has, source = block_source(block_map)
    parent_block = lax.axis_index("fr")
    present = has[parent_block]
    child_block = NPB + source[parent_block]
    rows = lax.dynamic_slice_in_dim(rest, child_block * BLK, BLK, 0)
    panel_rows = lax.dynamic_slice_in_dim(panel, child_block * BLK, BLK, 0)
    schur = rows - dot_t(panel_rows, panel[P_SIZE:])
    tiles = schur.reshape(BLK, NFB - NPB, BLK)
    placed = jnp.take(tiles, source[NPB:], axis=1)
    placed = jnp.where(has[None, NPB:, None] & present, placed, 0.0)
    return placed.reshape(BLK, (NFB - NPB) * BLK)


def parent(rest, panel, block_map, shares_full, level_bit):
    columns = extend_columns(rest, panel, block_map)
    own_rest = extend_own(rest, panel, block_map)
    columns = shares_full + (columns + partner(columns, "sub", level_bit))
    own_rest = own_rest + partner(own_rest, "sub", level_bit)
    return columns, own_rest


def local(front_leaf, shares_one, shares_two, map_leaf, map_mid):
    row_count = front_leaf.shape[0]
    row_start = lax.axis_index("fr") * row_count
    sub_index = lax.axis_index("sub")

    one_own = shares_one + partner(shares_one, "sub", 0)
    two_own = shares_two + partner(shares_two, "sub", 0)
    two_own = two_own + partner(two_own, "sub", 1)

    leaf = front_leaf.astype(jnp.float32)
    leaf_full = factor(gather_rows(leaf[:, :P_SIZE]))
    leaf_rest = gather_rows(leaf[:, P_SIZE:])
    one_full = gather_rows(one_own)
    leaf_panel = lax.dynamic_slice_in_dim(leaf_full, row_start, row_count, 0)

    middle_columns, middle_own = parent(leaf_rest, leaf_full, map_leaf[0], one_full, 0)
    middle_full = factor(middle_columns)
    middle_rest = gather_rows(middle_own)
    two_full = gather_rows(two_own)
    middle_panel = lax.dynamic_slice_in_dim(middle_full, row_start, row_count, 0)

    pair_map = lax.dynamic_index_in_dim(map_mid, sub_index // 2, 0, keepdims=False)
    top_columns, top_own = parent(middle_rest, middle_full, pair_map, two_full, 1)
    top_full = factor(top_columns)
    top_panel = lax.dynamic_slice_in_dim(top_full, row_start, row_count, 0)

    schur = top_own - dot_t(top_panel, top_full[P_SIZE:])
    row_ids = row_start + jnp.arange(row_count)
    contribution = jnp.where((row_ids >= P_SIZE)[:, None], schur, 0.0)
    return (leaf_panel, middle_panel, top_panel, contribution)


def solution(mesh):
    in_specs = (
        P(("sub", "fr"), None),
        P(("sub", "fr"), None),
        P(("sub", "fr"), None),
        P("sub", None),
        P(),
    )
    out_specs = (
        P(("sub", "fr"), None),
        P(("sub", "fr"), None),
        P(("sub", "fr"), None),
        P(("sub", "fr"), None),
    )
    return jax.shard_map(local, mesh=mesh, in_specs=in_specs, out_specs=out_specs, check_vma=False)
```

```python
import jax
import jax.numpy as jnp
from jax import lax
from jax.sharding import PartitionSpec as P

BLK = 128
P_SIZE = 384
NFB = 16
NPB = 3


HIGH = lax.Precision.HIGHEST


def partner(array, axis, stride):
    return lax.ppermute(array, axis, [(i, i ^ 1 << stride) for i in range(lax.axis_size(axis))])


def gather_rows(array):
    return lax.all_gather(array, "fr", axis=0, tiled=True)


def dot_t(left, right):
    return jnp.dot(left, right.T, precision=HIGH, preferred_element_type=jnp.float32)


def factor(columns):
    trailing = columns
    panels = []
    for block_index in range(NPB):
        block_low = block_index * BLK
        lower_block = jnp.tril(jnp.linalg.cholesky(trailing[:BLK, :BLK]))
        below = lax.linalg.triangular_solve(
            lower_block, trailing[BLK:, :BLK], left_side=False, lower=True, transpose_a=True
        )
        panels.append(
            jnp.concatenate(
                [jnp.zeros((block_low, BLK), jnp.float32), lower_block, below], axis=0
            )
        )
        if block_index < NPB - 1:
            width = trailing.shape[1] - BLK
            trailing = trailing[BLK:, BLK:] - dot_t(below, below[:width])
    return jnp.concatenate(panels, axis=1)


def block_source(block_map):
    match = block_map[None, :] == jnp.arange(NFB, dtype=jnp.int32)[:, None]
    return jnp.any(match, axis=1), jnp.argmax(match, axis=1).astype(jnp.int32)


def pick_rows(array, source):
    count = array.shape[0] // BLK
    tiles = array.reshape(count, BLK, array.shape[1])
    return jnp.take(tiles, source, axis=0).reshape(source.shape[0] * BLK, array.shape[1])


def pick_columns(array, source):
    return pick_rows(array.T, source).T


def child_columns(rest, panel, block_map):
    has, source = block_source(block_map)
    lower = panel[P_SIZE:]
    picked = jnp.concatenate(
        [lax.dynamic_slice(rest, (P_SIZE, source[f] * BLK), (rest.shape[1], BLK)) for f in range(NPB)],
        axis=1,
    )
    schur = picked - dot_t(lower, pick_rows(lower, source[:NPB]))
    return jnp.where(jnp.repeat(has[:NPB], BLK)[None, :], schur, 0.0)


def place_rows(schur, block_map):
    has, source = block_source(block_map)
    rows = pick_rows(schur, source)
    return jnp.where(jnp.repeat(has, BLK)[:, None], rows, 0.0)


def extend_own(rest, panel, block_map):
    has, source = block_source(block_map)
    parent_block = lax.axis_index("fr")
    present = has[parent_block]
    child_block = NPB + source[parent_block]
    rows = lax.dynamic_slice_in_dim(rest, child_block * BLK, BLK, 0)
    panel_rows = lax.dynamic_slice_in_dim(panel, child_block * BLK, BLK, 0)
    blocks = source[NPB:]
    schur = pick_columns(rows, blocks) - dot_t(panel_rows, pick_rows(panel[P_SIZE:], blocks))
    keep = jnp.repeat(has[NPB:], BLK)[None, :] & present
    return jnp.where(keep, schur, 0.0)


def parent(rest, panel, block_map, partner_map, shares_full, level_bit):
    schur = child_columns(rest, panel, block_map)
    own_rest = extend_own(rest, panel, block_map)
    columns = place_rows(schur, block_map) + place_rows(
        partner(schur, "sub", level_bit), partner_map
    )
    own_rest = own_rest + partner(own_rest, "sub", level_bit)
    return shares_full + columns, own_rest


def local(front_leaf, shares_one, shares_two, map_leaf, map_mid):
    row_count = front_leaf.shape[0]
    row_start = lax.axis_index("fr") * row_count
    sub_index = lax.axis_index("sub")

    one_own = shares_one + partner(shares_one, "sub", 0)
    two_own = shares_two + partner(shares_two, "sub", 0)
    two_own = two_own + partner(two_own, "sub", 1)

    leaf = front_leaf.astype(jnp.float32)
    leaf_full = factor(gather_rows(leaf[:, :P_SIZE]))
    leaf_rest = gather_rows(leaf[:, P_SIZE:])
    one_full = gather_rows(one_own)
    leaf_panel = lax.dynamic_slice_in_dim(leaf_full, row_start, row_count, 0)

    leaf_map = map_leaf[0]
    middle_columns, middle_own = parent(
        leaf_rest, leaf_full, leaf_map, partner(leaf_map, "sub", 0), one_full, 0
    )
    middle_full = factor(middle_columns)
    middle_rest = gather_rows(middle_own)
    two_full = gather_rows(two_own)
    middle_panel = lax.dynamic_slice_in_dim(middle_full, row_start, row_count, 0)

    pair_map = lax.dynamic_index_in_dim(map_mid, sub_index // 2, 0, keepdims=False)
    other_map = lax.dynamic_index_in_dim(map_mid, (sub_index ^ 2) // 2, 0, keepdims=False)
    top_columns, top_own = parent(middle_rest, middle_full, pair_map, other_map, two_full, 1)
    top_full = factor(top_columns)
    top_panel = lax.dynamic_slice_in_dim(top_full, row_start, row_count, 0)

    schur = top_own - dot_t(top_panel, top_full[P_SIZE:])
    row_ids = row_start + jnp.arange(row_count)
    contribution = jnp.where((row_ids >= P_SIZE)[:, None], schur, 0.0)
    return (leaf_panel, middle_panel, top_panel, contribution)


def solution(mesh):
    in_specs = (
        P(("sub", "fr"), None),
        P(("sub", "fr"), None),
        P(("sub", "fr"), None),
        P("sub", None),
        P(),
    )
    out_specs = (
        P(("sub", "fr"), None),
        P(("sub", "fr"), None),
        P(("sub", "fr"), None),
        P(("sub", "fr"), None),
    )
    return jax.shard_map(local, mesh=mesh, in_specs=in_specs, out_specs=out_specs, check_vma=False)
```

```python
import jax
import jax.numpy as jnp
from jax import lax
from jax.sharding import PartitionSpec as P

BLK = 128
P_SIZE = 384
NFB = 16
NPB = 3


HIGH = lax.Precision.HIGHEST


def partner(array, axis, stride):
    return lax.ppermute(array, axis, [(i, i ^ 1 << stride) for i in range(lax.axis_size(axis))])


def gather_rows(array):
    return lax.all_gather(array, "fr", axis=0, tiled=True)


def gather_rows_direct(array):
    count = lax.axis_size("fr")
    copies = jnp.broadcast_to(array[None], (count,) + array.shape)
    gathered = lax.all_to_all(copies, "fr", 0, 0, tiled=False)
    return gathered.reshape(count * array.shape[0], array.shape[1])


def dot_t(left, right, precision=HIGH):
    return jnp.dot(left, right.T, precision=precision, preferred_element_type=jnp.float32)


SCHUR = lax.Precision.HIGH


def factor(columns):
    trailing = columns
    panels = []
    for block_index in range(NPB):
        block_low = block_index * BLK
        lower_block = jnp.tril(jnp.linalg.cholesky(trailing[:BLK, :BLK]))
        below = lax.linalg.triangular_solve(
            lower_block, trailing[BLK:, :BLK], left_side=False, lower=True, transpose_a=True
        )
        panels.append(
            jnp.concatenate(
                [jnp.zeros((block_low, BLK), jnp.float32), lower_block, below], axis=0
            )
        )
        if block_index < NPB - 1:
            width = trailing.shape[1] - BLK
            trailing = trailing[BLK:, BLK:] - dot_t(below, below[:width])
    return jnp.concatenate(panels, axis=1)


def block_source(block_map):
    match = block_map[None, :] == jnp.arange(NFB, dtype=jnp.int32)[:, None]
    return jnp.any(match, axis=1), jnp.argmax(match, axis=1).astype(jnp.int32)


def padded_source(block_map):
    has, source = block_source(block_map)
    return jnp.where(has, source, NFB - NPB)


def pick_rows(array, source):
    count = array.shape[0] // BLK
    tiles = array.reshape(count, BLK, array.shape[1])
    return jnp.take(tiles, source, axis=0).reshape(source.shape[0] * BLK, array.shape[1])


def pick_columns(array, source):
    return pick_rows(array.T, source).T


def child_columns(rest, panel, block_map):
    has, source = block_source(block_map)
    lower = panel[P_SIZE:]
    picked = jnp.concatenate(
        [lax.dynamic_slice(rest, (P_SIZE, source[f] * BLK), (rest.shape[1], BLK)) for f in range(NPB)],
        axis=1,
    )
    schur = picked - dot_t(lower, pick_rows(lower, source[:NPB]), SCHUR)
    return jnp.where(jnp.repeat(has[:NPB], BLK)[None, :], schur, 0.0)


def place_rows(schur, block_map):
    padded = jnp.concatenate([schur, jnp.zeros((BLK, schur.shape[1]), jnp.float32)], axis=0)
    return pick_rows(padded, padded_source(block_map))


def extend_own(rest, panel, block_map):
    has, source = block_source(block_map)
    parent_block = lax.axis_index("fr")
    present = has[parent_block]
    child_block = NPB + source[parent_block]
    rows = lax.dynamic_slice_in_dim(rest, child_block * BLK, BLK, 0)
    panel_rows = lax.dynamic_slice_in_dim(panel, child_block * BLK, BLK, 0)
    blocks = source[NPB:]
    schur = pick_columns(rows, blocks) - dot_t(panel_rows, pick_rows(panel[P_SIZE:], blocks), SCHUR)
    keep = jnp.repeat(has[NPB:], BLK)[None, :] & present
    return jnp.where(keep, schur, 0.0)


def parent(rest, panel, block_map, partner_map, shares_full, level_bit):
    schur = child_columns(rest, panel, block_map)
    own_rest = extend_own(rest, panel, block_map)
    columns = place_rows(schur, block_map) + place_rows(
        partner(schur, "sub", level_bit), partner_map
    )
    own_rest = own_rest + partner(own_rest, "sub", level_bit)
    return shares_full + columns, own_rest


def local(front_leaf, shares_one, shares_two, map_leaf, map_mid):
    row_count = front_leaf.shape[0]
    row_start = lax.axis_index("fr") * row_count
    sub_index = lax.axis_index("sub")

    one_own = shares_one + partner(shares_one, "sub", 0)
    two_own = shares_two + partner(shares_two, "sub", 0)
    two_own = two_own + partner(two_own, "sub", 1)

    leaf = front_leaf.astype(jnp.float32)
    leaf_full = factor(gather_rows_direct(leaf[:, :P_SIZE]))
    leaf_rest = gather_rows(leaf[:, P_SIZE:])
    one_full = gather_rows(one_own)
    leaf_panel = lax.dynamic_slice_in_dim(leaf_full, row_start, row_count, 0)

    leaf_map = map_leaf[0]
    middle_columns, middle_own = parent(
        leaf_rest, leaf_full, leaf_map, partner(leaf_map, "sub", 0), one_full, 0
    )
    middle_full = factor(middle_columns)
    middle_rest = gather_rows(middle_own)
    two_full = gather_rows(two_own)
    middle_panel = lax.dynamic_slice_in_dim(middle_full, row_start, row_count, 0)

    pair_map = lax.dynamic_index_in_dim(map_mid, sub_index // 2, 0, keepdims=False)
    other_map = lax.dynamic_index_in_dim(map_mid, (sub_index ^ 2) // 2, 0, keepdims=False)
    top_columns, top_own = parent(middle_rest, middle_full, pair_map, other_map, two_full, 1)
    top_full = factor(top_columns)
    top_panel = lax.dynamic_slice_in_dim(top_full, row_start, row_count, 0)

    schur = top_own - dot_t(top_panel, top_full[P_SIZE:], SCHUR)
    row_ids = row_start + jnp.arange(row_count)
    contribution = jnp.where((row_ids >= P_SIZE)[:, None], schur, 0.0)
    return (leaf_panel, middle_panel, top_panel, contribution)


def solution(mesh):
    in_specs = (
        P(("sub", "fr"), None),
        P(("sub", "fr"), None),
        P(("sub", "fr"), None),
        P("sub", None),
        P(),
    )
    out_specs = (
        P(("sub", "fr"), None),
        P(("sub", "fr"), None),
        P(("sub", "fr"), None),
        P(("sub", "fr"), None),
    )
    return jax.shard_map(local, mesh=mesh, in_specs=in_specs, out_specs=out_specs, check_vma=False)
```

```python
import jax
import jax.numpy as jnp
from jax import lax
from jax.sharding import PartitionSpec as P

BLK = 128
P_SIZE = 384
NFB = 16
NPB = 3


HIGH = lax.Precision.HIGHEST


def partner(array, axis, stride):
    return lax.ppermute(array, axis, [(i, i ^ 1 << stride) for i in range(lax.axis_size(axis))])


def gather_rows(array):
    return lax.all_gather(array, "fr", axis=0, tiled=True)


def gather_rows_direct(array):
    count = lax.axis_size("fr")
    copies = jnp.broadcast_to(array[None], (count,) + array.shape)
    gathered = lax.all_to_all(copies, "fr", 0, 0, tiled=False)
    return gathered.reshape(count * array.shape[0], array.shape[1])


def dot_t(left, right, precision=HIGH):
    return jnp.dot(left, right.T, precision=precision, preferred_element_type=jnp.float32)


SCHUR = lax.Precision.HIGH


def factor(columns):
    trailing = columns
    panels = []
    for block_index in range(NPB):
        block_low = block_index * BLK
        lower_block = jnp.tril(jnp.linalg.cholesky(trailing[:BLK, :BLK]))
        below = lax.linalg.triangular_solve(
            lower_block, trailing[BLK:, :BLK], left_side=False, lower=True, transpose_a=True
        )
        panels.append(
            jnp.concatenate(
                [jnp.zeros((block_low, BLK), jnp.float32), lower_block, below], axis=0
            )
        )
        if block_index < NPB - 1:
            width = trailing.shape[1] - BLK
            trailing = trailing[BLK:, BLK:] - dot_t(below, below[:width])
    return jnp.concatenate(panels, axis=1)


def block_source(block_map):
    match = block_map[None, :] == jnp.arange(NFB, dtype=jnp.int32)[:, None]
    return jnp.any(match, axis=1), jnp.argmax(match, axis=1).astype(jnp.int32)


def padded_source(block_map):
    has, source = block_source(block_map)
    return jnp.where(has, source, NFB - NPB)


def pick_rows(array, source):
    count = array.shape[0] // BLK
    tiles = array.reshape(count, BLK, array.shape[1])
    return jnp.take(tiles, source, axis=0).reshape(source.shape[0] * BLK, array.shape[1])


def pick_columns(array, source):
    return pick_rows(array.T, source).T


def child_columns(rest, panel, block_map):
    has, source = block_source(block_map)
    lower = panel[P_SIZE:]
    picked = jnp.concatenate(
        [lax.dynamic_slice(rest, (P_SIZE, source[f] * BLK), (rest.shape[1], BLK)) for f in range(NPB)],
        axis=1,
    )
    schur = picked - dot_t(lower, pick_rows(lower, source[:NPB]), SCHUR)
    return jnp.where(jnp.repeat(has[:NPB], BLK)[None, :], schur, 0.0)


def place_rows(schur, block_map):
    padded = jnp.concatenate([schur, jnp.zeros((BLK, schur.shape[1]), jnp.float32)], axis=0)
    return pick_rows(padded, padded_source(block_map))


def extend_own(rest, panel, block_map):
    has, source = block_source(block_map)
    parent_block = lax.axis_index("fr")
    present = has[parent_block]
    child_block = NPB + source[parent_block]
    rows = lax.dynamic_slice_in_dim(rest, child_block * BLK, BLK, 0)
    panel_rows = lax.dynamic_slice_in_dim(panel, child_block * BLK, BLK, 0)
    blocks = source[NPB:]
    schur = pick_columns(rows, blocks) - dot_t(panel_rows, pick_rows(panel[P_SIZE:], blocks), SCHUR)
    keep = jnp.repeat(has[NPB:], BLK)[None, :] & present
    return jnp.where(keep, schur, 0.0)


def exchange(array, level_bit):
    if level_bit == 0:
        return partner(array, "sub", 0)
    half = array.shape[0] // 2
    core = lax.axis_index("sub") % 2
    mine = lax.dynamic_slice_in_dim(array, core * half, half, 0)
    received = partner(mine, "sub", level_bit)
    other = partner(received, "sub", 0)
    return jnp.where(
        core == 0,
        jnp.concatenate([received, other], axis=0),
        jnp.concatenate([other, received], axis=0),
    )


def parent(rest, panel, block_map, partner_map, shares_full, level_bit):
    schur = child_columns(rest, panel, block_map)
    own_rest = extend_own(rest, panel, block_map)
    columns = place_rows(schur, block_map) + place_rows(exchange(schur, level_bit), partner_map)
    own_rest = own_rest + exchange(own_rest, level_bit)
    return shares_full + columns, own_rest


def local(front_leaf, shares_one, shares_two, map_leaf, map_mid):
    row_count = front_leaf.shape[0]
    row_start = lax.axis_index("fr") * row_count
    sub_index = lax.axis_index("sub")

    one_own = shares_one + partner(shares_one, "sub", 0)
    two_own = shares_two + partner(shares_two, "sub", 0)
    two_own = two_own + partner(two_own, "sub", 1)

    leaf = front_leaf.astype(jnp.float32)
    leaf_full = factor(gather_rows_direct(leaf[:, :P_SIZE]))
    leaf_rest = gather_rows(leaf[:, P_SIZE:])
    one_full = gather_rows(one_own)
    leaf_panel = lax.dynamic_slice_in_dim(leaf_full, row_start, row_count, 0)

    leaf_map = map_leaf[0]
    middle_columns, middle_own = parent(
        leaf_rest, leaf_full, leaf_map, partner(leaf_map, "sub", 0), one_full, 0
    )
    middle_full = factor(middle_columns)
    middle_rest = gather_rows(middle_own)
    two_full = gather_rows(two_own)
    middle_panel = lax.dynamic_slice_in_dim(middle_full, row_start, row_count, 0)

    pair_map = lax.dynamic_index_in_dim(map_mid, sub_index // 2, 0, keepdims=False)
    other_map = lax.dynamic_index_in_dim(map_mid, (sub_index ^ 2) // 2, 0, keepdims=False)
    top_columns, top_own = parent(middle_rest, middle_full, pair_map, other_map, two_full, 1)
    top_full = factor(top_columns)
    top_panel = lax.dynamic_slice_in_dim(top_full, row_start, row_count, 0)

    schur = top_own - dot_t(top_panel, top_full[P_SIZE:], SCHUR)
    row_ids = row_start + jnp.arange(row_count)
    contribution = jnp.where((row_ids >= P_SIZE)[:, None], schur, 0.0)
    return (leaf_panel, middle_panel, top_panel, contribution)


def solution(mesh):
    in_specs = (
        P(("sub", "fr"), None),
        P(("sub", "fr"), None),
        P(("sub", "fr"), None),
        P("sub", None),
        P(),
    )
    out_specs = (
        P(("sub", "fr"), None),
        P(("sub", "fr"), None),
        P(("sub", "fr"), None),
        P(("sub", "fr"), None),
    )
    return jax.shard_map(local, mesh=mesh, in_specs=in_specs, out_specs=out_specs, check_vma=False)
```

```python
import jax
import jax.numpy as jnp
from jax import lax
from jax.sharding import PartitionSpec as P

BLK = 128
P_SIZE = 384
NFB = 16
NPB = 3


HIGH = lax.Precision.HIGHEST


def partner(array, axis, stride):
    return lax.ppermute(array, axis, [(i, i ^ 1 << stride) for i in range(lax.axis_size(axis))])


def gather_rows(array):
    return lax.all_gather(array, "fr", axis=0, tiled=True)


def gather_rows_direct(array):
    count = lax.axis_size("fr")
    copies = jnp.broadcast_to(array[None], (count,) + array.shape)
    gathered = lax.all_to_all(copies, "fr", 0, 0, tiled=False)
    return gathered.reshape(count * array.shape[0], array.shape[1])


def dot_t(left, right, precision=HIGH):
    return jnp.dot(left, right.T, precision=precision, preferred_element_type=jnp.float32)


SCHUR = lax.Precision.HIGH


def factor(columns):
    trailing = columns
    panels = []
    for block_index in range(NPB):
        block_low = block_index * BLK
        lower_block = jnp.tril(jnp.linalg.cholesky(trailing[:BLK, :BLK]))
        below = lax.linalg.triangular_solve(
            lower_block, trailing[BLK:, :BLK], left_side=False, lower=True, transpose_a=True
        )
        panels.append(
            jnp.concatenate(
                [jnp.zeros((block_low, BLK), jnp.float32), lower_block, below], axis=0
            )
        )
        if block_index < NPB - 1:
            width = trailing.shape[1] - BLK
            trailing = trailing[BLK:, BLK:] - dot_t(below, below[:width], SCHUR)
    return jnp.concatenate(panels, axis=1)


def block_source(block_map):
    match = block_map[None, :] == jnp.arange(NFB, dtype=jnp.int32)[:, None]
    return jnp.any(match, axis=1), jnp.argmax(match, axis=1).astype(jnp.int32)


def padded_source(block_map):
    has, source = block_source(block_map)
    return jnp.where(has, source, NFB - NPB)


def pick_rows(array, source):
    count = array.shape[0] // BLK
    tiles = array.reshape(count, BLK, array.shape[1])
    picked = jnp.take(tiles, source, axis=0, mode="fill", fill_value=0.0)
    return picked.reshape(source.shape[0] * BLK, array.shape[1])


def pick_columns(array, source):
    return pick_rows(array.T, source).T


def child_columns(rest, panel, block_map):
    has, source = block_source(block_map)
    lower = panel[P_SIZE:]
    picked = jnp.concatenate(
        [lax.dynamic_slice(rest, (P_SIZE, source[f] * BLK), (rest.shape[1], BLK)) for f in range(NPB)],
        axis=1,
    )
    picked = jnp.where(jnp.repeat(has[:NPB], BLK)[None, :], picked, 0.0)
    return picked - dot_t(lower, pick_rows(lower, padded_source(block_map)[:NPB]), SCHUR)


def place_rows(schur, block_map):
    return pick_rows(schur, padded_source(block_map))


def extend_own(rest, panel, block_map):
    has, source = block_source(block_map)
    parent_block = lax.axis_index("fr")
    present = has[parent_block]
    child_block = NPB + source[parent_block]
    rows = lax.dynamic_slice_in_dim(rest, child_block * BLK, BLK, 0)
    panel_rows = lax.dynamic_slice_in_dim(panel, child_block * BLK, BLK, 0)
    blocks = source[NPB:]
    schur = pick_columns(rows, blocks) - dot_t(panel_rows, pick_rows(panel[P_SIZE:], blocks), SCHUR)
    keep = jnp.repeat(has[NPB:], BLK)[None, :] & present
    return jnp.where(keep, schur, 0.0)


def exchange(array, level_bit):
    if level_bit == 0:
        return partner(array, "sub", 0)
    half = array.shape[0] // 2
    core = lax.axis_index("sub") % 2
    mine = lax.dynamic_slice_in_dim(array, core * half, half, 0)
    received = partner(mine, "sub", level_bit)
    other = partner(received, "sub", 0)
    return jnp.where(
        core == 0,
        jnp.concatenate([received, other], axis=0),
        jnp.concatenate([other, received], axis=0),
    )


def parent(rest, panel, block_map, partner_map, shares_full, level_bit):
    schur = child_columns(rest, panel, block_map)
    own_rest = extend_own(rest, panel, block_map)
    columns = place_rows(schur, block_map) + place_rows(exchange(schur, level_bit), partner_map)
    own_rest = own_rest + exchange(own_rest, level_bit)
    return shares_full + columns, own_rest


def local(front_leaf, shares_one, shares_two, map_leaf, map_mid):
    row_count = front_leaf.shape[0]
    row_start = lax.axis_index("fr") * row_count
    sub_index = lax.axis_index("sub")

    one_own = shares_one + partner(shares_one, "sub", 0)
    two_own = shares_two + partner(shares_two, "sub", 0)
    two_own = two_own + partner(two_own, "sub", 1)

    leaf = front_leaf.astype(jnp.float32)
    leaf_full = factor(gather_rows_direct(leaf[:, :P_SIZE]))
    leaf_rest = gather_rows(leaf[:, P_SIZE:])
    one_full = gather_rows(one_own)
    leaf_panel = lax.dynamic_slice_in_dim(leaf_full, row_start, row_count, 0)

    leaf_map = map_leaf[0]
    middle_columns, middle_own = parent(
        leaf_rest, leaf_full, leaf_map, partner(leaf_map, "sub", 0), one_full, 0
    )
    middle_full = factor(middle_columns)
    middle_rest = gather_rows(middle_own)
    two_full = gather_rows(two_own)
    middle_panel = lax.dynamic_slice_in_dim(middle_full, row_start, row_count, 0)

    pair_map = lax.dynamic_index_in_dim(map_mid, sub_index // 2, 0, keepdims=False)
    other_map = lax.dynamic_index_in_dim(map_mid, (sub_index ^ 2) // 2, 0, keepdims=False)
    top_columns, top_own = parent(middle_rest, middle_full, pair_map, other_map, two_full, 1)
    top_full = factor(top_columns)
    top_panel = lax.dynamic_slice_in_dim(top_full, row_start, row_count, 0)

    schur = top_own - dot_t(top_panel, top_full[P_SIZE:], SCHUR)
    row_ids = row_start + jnp.arange(row_count)
    contribution = jnp.where((row_ids >= P_SIZE)[:, None], schur, 0.0)
    return (leaf_panel, middle_panel, top_panel, contribution)


def solution(mesh):
    in_specs = (
        P(("sub", "fr"), None),
        P(("sub", "fr"), None),
        P(("sub", "fr"), None),
        P("sub", None),
        P(),
    )
    out_specs = (
        P(("sub", "fr"), None),
        P(("sub", "fr"), None),
        P(("sub", "fr"), None),
        P(("sub", "fr"), None),
    )
    return jax.shard_map(local, mesh=mesh, in_specs=in_specs, out_specs=out_specs, check_vma=False)
```

```python
import jax
import jax.numpy as jnp
from jax import lax
from jax.sharding import PartitionSpec as P

BLK = 128
P_SIZE = 384
NFB = 16
NPB = 3


HIGH = lax.Precision.HIGHEST


def partner(array, axis, stride):
    return lax.ppermute(array, axis, [(i, i ^ 1 << stride) for i in range(lax.axis_size(axis))])


def gather_rows(array):
    return lax.all_gather(array, "fr", axis=0, tiled=True)


def gather_rows_direct(array):
    count = lax.axis_size("fr")
    copies = jnp.broadcast_to(array[None], (count,) + array.shape)
    gathered = lax.all_to_all(copies, "fr", 0, 0, tiled=False)
    return gathered.reshape(count * array.shape[0], array.shape[1])


def dot_t(left, right, precision=HIGH):
    return jnp.dot(left, right.T, precision=precision, preferred_element_type=jnp.float32)


SCHUR = lax.Precision.HIGH


def factor(columns):
    trailing = columns
    panels = []
    for block_index in range(NPB):
        block_low = block_index * BLK
        lower_block = jnp.tril(jnp.linalg.cholesky(trailing[:BLK, :BLK]))
        below = lax.linalg.triangular_solve(
            lower_block, trailing[BLK:, :BLK], left_side=False, lower=True, transpose_a=True
        )
        panels.append(
            jnp.concatenate(
                [jnp.zeros((block_low, BLK), jnp.float32), lower_block, below], axis=0
            )
        )
        if block_index < NPB - 1:
            width = trailing.shape[1] - BLK
            trailing = trailing[BLK:, BLK:] - dot_t(below, below[:width], SCHUR)
    return jnp.concatenate(panels, axis=1)


def block_source(block_map):
    match = block_map[None, :] == jnp.arange(NFB, dtype=jnp.int32)[:, None]
    return jnp.any(match, axis=1), jnp.argmax(match, axis=1).astype(jnp.int32)


def padded_source(block_map):
    has, source = block_source(block_map)
    return jnp.where(has, source, NFB - NPB)


def pick_rows(array, source):
    count = array.shape[0] // BLK
    tiles = array.reshape(count, BLK, array.shape[1])
    picked = jnp.take(tiles, source, axis=0, mode="fill", fill_value=0.0)
    return picked.reshape(source.shape[0] * BLK, array.shape[1])


def pick_columns(array, source):
    return pick_rows(array.T, source).T


def child_columns(rest, panel, block_map):
    has, source = block_source(block_map)
    lower = panel[P_SIZE:]
    picked = jnp.concatenate(
        [lax.dynamic_slice(rest, (P_SIZE, source[f] * BLK), (rest.shape[1], BLK)) for f in range(NPB)],
        axis=1,
    )
    picked = jnp.where(jnp.repeat(has[:NPB], BLK)[None, :], picked, 0.0)
    return picked - dot_t(lower, pick_rows(lower, padded_source(block_map)[:NPB]), SCHUR)


def place_rows(schur, block_map):
    return pick_rows(schur, padded_source(block_map))


def extend_own(rest, panel, block_map):
    has, source = block_source(block_map)
    parent_block = lax.axis_index("fr")
    present = has[parent_block]
    child_block = NPB + source[parent_block]
    rows = lax.dynamic_slice_in_dim(rest, child_block * BLK, BLK, 0)
    panel_rows = lax.dynamic_slice_in_dim(panel, child_block * BLK, BLK, 0)
    schur = rows - dot_t(panel_rows, panel[P_SIZE:], SCHUR)
    placed = pick_columns(schur, padded_source(block_map)[NPB:])
    return jnp.where(present, placed, 0.0)


def exchange(array, level_bit):
    if level_bit == 0:
        return partner(array, "sub", 0)
    half = array.shape[0] // 2
    core = lax.axis_index("sub") % 2
    mine = lax.dynamic_slice_in_dim(array, core * half, half, 0)
    received = partner(mine, "sub", level_bit)
    other = partner(received, "sub", 0)
    return jnp.where(
        core == 0,
        jnp.concatenate([received, other], axis=0),
        jnp.concatenate([other, received], axis=0),
    )


def parent(rest, panel, block_map, partner_map, shares_full, level_bit):
    schur = child_columns(rest, panel, block_map)
    own_rest = extend_own(rest, panel, block_map)
    columns = place_rows(schur, block_map) + place_rows(exchange(schur, level_bit), partner_map)
    own_rest = own_rest + exchange(own_rest, level_bit)
    return shares_full + columns, own_rest


def local(front_leaf, shares_one, shares_two, map_leaf, map_mid):
    row_count = front_leaf.shape[0]
    row_start = lax.axis_index("fr") * row_count
    sub_index = lax.axis_index("sub")

    one_own = shares_one + partner(shares_one, "sub", 0)
    two_own = shares_two + partner(shares_two, "sub", 0)
    two_own = two_own + partner(two_own, "sub", 1)

    leaf = front_leaf.astype(jnp.float32)
    leaf_full = factor(gather_rows_direct(leaf[:, :P_SIZE]))
    leaf_rest = gather_rows(leaf[:, P_SIZE:])
    one_full = gather_rows(one_own)
    leaf_panel = lax.dynamic_slice_in_dim(leaf_full, row_start, row_count, 0)

    leaf_map = map_leaf[0]
    middle_columns, middle_own = parent(
        leaf_rest, leaf_full, leaf_map, partner(leaf_map, "sub", 0), one_full, 0
    )
    middle_full = factor(middle_columns)
    middle_rest = gather_rows(middle_own)
    two_full = gather_rows(two_own)
    middle_panel = lax.dynamic_slice_in_dim(middle_full, row_start, row_count, 0)

    pair_map = lax.dynamic_index_in_dim(map_mid, sub_index // 2, 0, keepdims=False)
    other_map = lax.dynamic_index_in_dim(map_mid, (sub_index ^ 2) // 2, 0, keepdims=False)
    top_columns, top_own = parent(middle_rest, middle_full, pair_map, other_map, two_full, 1)
    top_full = factor(top_columns)
    top_panel = lax.dynamic_slice_in_dim(top_full, row_start, row_count, 0)

    schur = top_own - dot_t(top_panel, top_full[P_SIZE:], SCHUR)
    row_ids = row_start + jnp.arange(row_count)
    contribution = jnp.where((row_ids >= P_SIZE)[:, None], schur, 0.0)
    return (leaf_panel, middle_panel, top_panel, contribution)


def solution(mesh):
    in_specs = (
        P(("sub", "fr"), None),
        P(("sub", "fr"), None),
        P(("sub", "fr"), None),
        P("sub", None),
        P(),
    )
    out_specs = (
        P(("sub", "fr"), None),
        P(("sub", "fr"), None),
        P(("sub", "fr"), None),
        P(("sub", "fr"), None),
    )
    return jax.shard_map(local, mesh=mesh, in_specs=in_specs, out_specs=out_specs, check_vma=False)
```

```python
import jax
import jax.numpy as jnp
from jax import lax
from jax.sharding import PartitionSpec as P

BLK = 128
P_SIZE = 384
NFB = 16
NPB = 3


HIGH = lax.Precision.HIGHEST


def partner(array, axis, stride):
    return lax.ppermute(array, axis, [(i, i ^ 1 << stride) for i in range(lax.axis_size(axis))])


def gather_rows(array):
    return lax.all_gather(array, "fr", axis=0, tiled=True)


def gather_rows_direct(array):
    count = lax.axis_size("fr")
    copies = jnp.broadcast_to(array[None], (count,) + array.shape)
    gathered = lax.all_to_all(copies, "fr", 0, 0, tiled=False)
    return gathered.reshape(count * array.shape[0], array.shape[1])


def dot_t(left, right, precision=HIGH):
    return jnp.dot(left, right.T, precision=precision, preferred_element_type=jnp.float32)


SCHUR = lax.Precision.HIGH


def factor(columns):
    trailing = columns
    panels = []
    for block_index in range(NPB):
        block_low = block_index * BLK
        lower_block = jnp.tril(jnp.linalg.cholesky(trailing[:BLK, :BLK]))
        below = lax.linalg.triangular_solve(
            lower_block, trailing[BLK:, :BLK], left_side=False, lower=True, transpose_a=True
        )
        panels.append(
            jnp.concatenate(
                [jnp.zeros((block_low, BLK), jnp.float32), lower_block, below], axis=0
            )
        )
        if block_index < NPB - 1:
            width = trailing.shape[1] - BLK
            trailing = trailing[BLK:, BLK:] - dot_t(below, below[:width], SCHUR)
    return jnp.concatenate(panels, axis=1)


def block_source(block_map):
    match = block_map[None, :] == jnp.arange(NFB, dtype=jnp.int32)[:, None]
    return jnp.any(match, axis=1), jnp.argmax(match, axis=1).astype(jnp.int32)


def padded_source(block_map):
    has, source = block_source(block_map)
    return jnp.where(has, source, NFB - NPB)


def pick_rows(array, source):
    count = array.shape[0] // BLK
    tiles = array.reshape(count, BLK, array.shape[1])
    picked = jnp.take(tiles, source, axis=0, mode="fill", fill_value=0.0)
    return picked.reshape(source.shape[0] * BLK, array.shape[1])


def pick_columns(array, source):
    return pick_rows(array.T, source).T


def child_columns(rest, panel, block_map):
    has, source = block_source(block_map)
    picked = jnp.concatenate(
        [lax.dynamic_slice(rest, (P_SIZE, source[f] * BLK), (rest.shape[1], BLK)) for f in range(NPB)],
        axis=1,
    )
    picked = jnp.where(jnp.repeat(has[:NPB], BLK)[None, :], picked, 0.0)
    picked_panel = pick_rows(panel, NPB + padded_source(block_map)[:NPB])
    return picked - dot_t(panel, picked_panel, SCHUR)[P_SIZE:]


def place_rows(schur, block_map):
    return pick_rows(schur, padded_source(block_map))


def extend_own(rest, panel, block_map):
    has, source = block_source(block_map)
    parent_block = lax.axis_index("fr")
    present = has[parent_block]
    child_block = NPB + source[parent_block]
    rows = lax.dynamic_slice_in_dim(rest, child_block * BLK, BLK, 0)
    panel_rows = lax.dynamic_slice_in_dim(panel, child_block * BLK, BLK, 0)
    schur = rows - dot_t(panel_rows, panel, SCHUR)[:, P_SIZE:]
    placed = pick_columns(schur, padded_source(block_map)[NPB:])
    return jnp.where(present, placed, 0.0)


def exchange(array, level_bit):
    if level_bit == 0:
        return partner(array, "sub", 0)
    half = array.shape[0] // 2
    core = lax.axis_index("sub") % 2
    mine = lax.dynamic_slice_in_dim(array, core * half, half, 0)
    received = partner(mine, "sub", level_bit)
    other = partner(received, "sub", 0)
    return jnp.where(
        core == 0,
        jnp.concatenate([received, other], axis=0),
        jnp.concatenate([other, received], axis=0),
    )


def parent(rest, panel, block_map, partner_map, shares_full, level_bit):
    schur = child_columns(rest, panel, block_map)
    own_rest = extend_own(rest, panel, block_map)
    columns = place_rows(schur, block_map) + place_rows(exchange(schur, level_bit), partner_map)
    own_rest = own_rest + exchange(own_rest, level_bit)
    return shares_full + columns, own_rest


def local(front_leaf, shares_one, shares_two, map_leaf, map_mid):
    row_count = front_leaf.shape[0]
    row_start = lax.axis_index("fr") * row_count
    sub_index = lax.axis_index("sub")

    one_own = shares_one + partner(shares_one, "sub", 0)
    two_own = shares_two + partner(shares_two, "sub", 0)
    two_own = two_own + partner(two_own, "sub", 1)

    leaf = front_leaf.astype(jnp.float32)
    leaf_full = factor(gather_rows_direct(leaf[:, :P_SIZE]))
    leaf_rest = gather_rows(leaf[:, P_SIZE:])
    one_full = gather_rows(one_own)
    leaf_panel = lax.dynamic_slice_in_dim(leaf_full, row_start, row_count, 0)

    leaf_map = map_leaf[0]
    middle_columns, middle_own = parent(
        leaf_rest, leaf_full, leaf_map, partner(leaf_map, "sub", 0), one_full, 0
    )
    middle_full = factor(middle_columns)
    middle_rest = gather_rows(middle_own)
    two_full = gather_rows(two_own)
    middle_panel = lax.dynamic_slice_in_dim(middle_full, row_start, row_count, 0)

    pair_map = lax.dynamic_index_in_dim(map_mid, sub_index // 2, 0, keepdims=False)
    other_map = lax.dynamic_index_in_dim(map_mid, (sub_index ^ 2) // 2, 0, keepdims=False)
    top_columns, top_own = parent(middle_rest, middle_full, pair_map, other_map, two_full, 1)
    top_full = factor(top_columns)
    top_panel = lax.dynamic_slice_in_dim(top_full, row_start, row_count, 0)

    schur = top_own - dot_t(top_panel, top_full[P_SIZE:], SCHUR)
    row_ids = row_start + jnp.arange(row_count)
    contribution = jnp.where((row_ids >= P_SIZE)[:, None], schur, 0.0)
    return (leaf_panel, middle_panel, top_panel, contribution)


def solution(mesh):
    in_specs = (
        P(("sub", "fr"), None),
        P(("sub", "fr"), None),
        P(("sub", "fr"), None),
        P("sub", None),
        P(),
    )
    out_specs = (
        P(("sub", "fr"), None),
        P(("sub", "fr"), None),
        P(("sub", "fr"), None),
        P(("sub", "fr"), None),
    )
    return jax.shard_map(local, mesh=mesh, in_specs=in_specs, out_specs=out_specs, check_vma=False)
```

```python
import jax
import jax.numpy as jnp
from jax import lax
from jax.sharding import PartitionSpec as P

BLK = 128
P_SIZE = 384
NFB = 16
NPB = 3


HIGH = lax.Precision.HIGHEST


def partner(array, axis, stride):
    return lax.ppermute(array, axis, [(i, i ^ 1 << stride) for i in range(lax.axis_size(axis))])


def gather_rows(array):
    return lax.all_gather(array, "fr", axis=0, tiled=True)


def gather_rows_direct(array):
    count = lax.axis_size("fr")
    copies = jnp.broadcast_to(array[None], (count,) + array.shape)
    gathered = lax.all_to_all(copies, "fr", 0, 0, tiled=False)
    return gathered.reshape(count * array.shape[0], array.shape[1])


def dot_t(left, right, precision=HIGH):
    return jnp.dot(left, right.T, precision=precision, preferred_element_type=jnp.float32)


SCHUR = lax.Precision.HIGH


def factor(columns):
    trailing = columns
    panels = []
    for block_index in range(NPB):
        block_low = block_index * BLK
        lower_block = jnp.tril(jnp.linalg.cholesky(trailing[:BLK, :BLK]))
        below = lax.linalg.triangular_solve(
            lower_block, trailing[BLK:, :BLK], left_side=False, lower=True, transpose_a=True
        )
        panels.append(
            jnp.concatenate(
                [jnp.zeros((block_low, BLK), jnp.float32), lower_block, below], axis=0
            )
        )
        if block_index < NPB - 1:
            width = trailing.shape[1] - BLK
            trailing = trailing[BLK:, BLK:] - dot_t(below, below[:width], SCHUR)
    return jnp.concatenate(panels, axis=1)


def block_source(block_map):
    match = block_map[None, :] == jnp.arange(NFB, dtype=jnp.int32)[:, None]
    return jnp.any(match, axis=1), jnp.argmax(match, axis=1).astype(jnp.int32)


def padded_source(block_map):
    has, source = block_source(block_map)
    return jnp.where(has, source, NFB - NPB)


def pick_rows(array, source):
    count = array.shape[0] // BLK
    tiles = array.reshape(count, BLK, array.shape[1])
    picked = jnp.take(tiles, source, axis=0, mode="fill", fill_value=0.0)
    return picked.reshape(source.shape[0] * BLK, array.shape[1])


def pick_columns(array, source):
    return pick_rows(array.T, source).T


def child_columns(rest, panel, block_map):
    has, source = block_source(block_map)
    picked = jnp.concatenate(
        [lax.dynamic_slice(rest, (P_SIZE, source[f] * BLK), (rest.shape[1], BLK)) for f in range(NPB)],
        axis=1,
    )
    picked = jnp.where(jnp.repeat(has[:NPB], BLK)[None, :], picked, 0.0)
    picked_panel = pick_rows(panel, NPB + padded_source(block_map)[:NPB])
    return picked - dot_t(panel, picked_panel, SCHUR)[P_SIZE:]


def place_rows(schur, block_map):
    return pick_rows(schur, padded_source(block_map))


def extend_own(rest, panel, block_map):
    has, source = block_source(block_map)
    parent_block = lax.axis_index("fr")
    present = has[parent_block]
    child_block = NPB + source[parent_block]
    rows = lax.dynamic_slice_in_dim(rest, child_block * BLK, BLK, 0)
    panel_rows = lax.dynamic_slice_in_dim(panel, child_block * BLK, BLK, 0)
    schur = rows - dot_t(panel_rows, panel, SCHUR)[:, P_SIZE:]
    return pick_columns(schur, jnp.where(present, padded_source(block_map)[NPB:], NFB - NPB))


def exchange(array, level_bit):
    if level_bit == 0:
        return partner(array, "sub", 0)
    half = array.shape[0] // 2
    core = lax.axis_index("sub") % 2
    mine = lax.dynamic_slice_in_dim(array, core * half, half, 0)
    received = partner(mine, "sub", level_bit)
    other = partner(received, "sub", 0)
    return jnp.where(
        core == 0,
        jnp.concatenate([received, other], axis=0),
        jnp.concatenate([other, received], axis=0),
    )


def parent(rest, panel, block_map, partner_map, shares_full, level_bit):
    schur = child_columns(rest, panel, block_map)
    own_rest = extend_own(rest, panel, block_map)
    columns = place_rows(schur, block_map) + place_rows(exchange(schur, level_bit), partner_map)
    own_rest = own_rest + exchange(own_rest, level_bit)
    return shares_full + columns, own_rest


def local(front_leaf, shares_one, shares_two, map_leaf, map_mid):
    row_count = front_leaf.shape[0]
    row_start = lax.axis_index("fr") * row_count
    sub_index = lax.axis_index("sub")

    one_own = shares_one + partner(shares_one, "sub", 0)
    two_own = shares_two + partner(shares_two, "sub", 0)
    two_own = two_own + partner(two_own, "sub", 1)

    leaf = front_leaf.astype(jnp.float32)
    leaf_full = factor(gather_rows_direct(leaf[:, :P_SIZE]))
    leaf_rest = gather_rows(leaf[:, P_SIZE:])
    one_full = gather_rows(one_own)
    leaf_panel = lax.dynamic_slice_in_dim(leaf_full, row_start, row_count, 0)

    leaf_map = map_leaf[0]
    middle_columns, middle_own = parent(
        leaf_rest, leaf_full, leaf_map, partner(leaf_map, "sub", 0), one_full, 0
    )
    middle_full = factor(middle_columns)
    middle_rest = gather_rows(middle_own)
    two_full = gather_rows(two_own)
    middle_panel = lax.dynamic_slice_in_dim(middle_full, row_start, row_count, 0)

    pair_map = lax.dynamic_index_in_dim(map_mid, sub_index // 2, 0, keepdims=False)
    other_map = lax.dynamic_index_in_dim(map_mid, (sub_index ^ 2) // 2, 0, keepdims=False)
    top_columns, top_own = parent(middle_rest, middle_full, pair_map, other_map, two_full, 1)
    top_full = factor(top_columns)
    top_panel = lax.dynamic_slice_in_dim(top_full, row_start, row_count, 0)

    schur = top_own - dot_t(top_panel, top_full, SCHUR)[:, P_SIZE:]
    row_ids = row_start + jnp.arange(row_count)
    contribution = jnp.where((row_ids >= P_SIZE)[:, None], schur, 0.0)
    return (leaf_panel, middle_panel, top_panel, contribution)


def solution(mesh):
    in_specs = (
        P(("sub", "fr"), None),
        P(("sub", "fr"), None),
        P(("sub", "fr"), None),
        P("sub", None),
        P(),
    )
    out_specs = (
        P(("sub", "fr"), None),
        P(("sub", "fr"), None),
        P(("sub", "fr"), None),
        P(("sub", "fr"), None),
    )
    return jax.shard_map(local, mesh=mesh, in_specs=in_specs, out_specs=out_specs, check_vma=False)
```
